256 devices in a mesh: dp: 4 (over x), expert: 64 (over z, y, core).
Axes of the slice: x: 4, y: 4, z: 8, core: 2. Of those that a mesh axis runs over, the one named last changes fastest.
Arguments:
- tokens: bfloat16 [32768, 4096], P(('dp', 'expert')), may hold values from -6 to 6
- out_grad: bfloat16 [32768, 4096], P(('dp', 'expert')), may hold values from -0.75 to 0.75
- routes: int32 [32768, 1], P(('dp', 'expert')), may hold values from 0 to 63; in each aligned block of 128 rows (0 to 127, 128 to 255, ...) at most 3 rows name the same one
- gate_probs: bfloat16 [32768, 1], P(('dp', 'expert')), may hold values from 0.049804688 to 1
- w_gate: bfloat16 [64, 4096, 768], P('expert', None, 'dp'), may hold values from -0.09375 to 0.09375
- w_up: bfloat16 [64, 4096, 768], P('expert', None, 'dp'), may hold values from -0.09375 to 0.09375
- w_down: bfloat16 [64, 768, 4096], P('expert', 'dp'), may hold values from -0.21875 to 0.21875
Outputs:
- grad_tokens: bfloat16 [32768, 4096], P(('dp', 'expert'))
- grad_probs: bfloat16 [32768, 1], P(('dp', 'expert'))
- grad_w_gate: bfloat16 [64, 4096, 768], P('expert', None, 'dp')
- grad_w_up: bfloat16 [64, 4096, 768], P('expert', None, 'dp')
- grad_w_down: bfloat16 [64, 768, 4096], P('expert', 'dp')
The draws below stay inside these ranges and needn't reach their ends.
Inputs may be any that keep to these rules, and one draw needn't show every extreme that they name: `routes`: the experts of one token are different. Among the 128 tokens of one device no expert is named more than 3 times, a bound that some block reaches.
All inputs are finite; a program needn't handle non-finite values.
Results may differ from the reference program's by a relative error of at most 0.018.
Values may be sent and summed in bfloat16 or wider, within the bound.
No kernel may reach another device: no remote copies, remote signals or barrier semaphores. Data moves between devices by JAX's collectives and lax.ppermute only.
A program may use at most 128 MiB of HBM per device.

```python
import math
import jax
import jax.numpy as jnp
import numpy as np
from jax import lax

D = 4096
H = 768
TOP = 1
TOK_DEV = 128
EXPERTS = 64
TOKENS = 32768
CAP = 3
N_DP = 4


def shard_levels(own_key, extent, cuts, least, largest):
    gain, own = 1.0, jax.random.fold_in(own_key, 6)
    for axis_at, shards_of in cuts:
        heights = jnp.exp(jax.random.uniform(jax.random.fold_in(own, axis_at), (shards_of,), jnp.float32, least / len(cuts), largest / len(cuts)))
        gain = gain * jnp.repeat(heights, extent[axis_at] // shards_of).reshape([-1 if axis == axis_at else 1 for axis in range(len(extent))])
    return gain


def routed_block(key, own, number, rows, count, top, most, lean):
    ranking = jax.random.permutation(key, count)
    packed, usual = shares(count, rows * top, most, lean, True), shares(count, rows * top, most, lean, False)
    places = jnp.arange(count)

    def named(lengths, rotation):
        used = int((lengths > 0).sum())
        fixed = max(1, used // 4)
        shifted = fixed + (places - fixed + rotation * (used - fixed)) % max(1, count - fixed)
        return jnp.zeros((count,), jnp.int32).at[ranking[jnp.where(places < fixed, places, shifted)]].set(jnp.asarray(lengths, jnp.int32))

    lengths = jnp.where(number % 4 == 0, named(packed, number // 4), named(usual, number - number // 4 - 1))
    mixed = jax.random.permutation(jax.random.fold_in(own, 3), count)
    donor, receiver = mixed[0:count // 2 * 2:2], mixed[1:count // 2 * 2:2]
    slack = jnp.minimum(lengths[donor] - 1, most - lengths[receiver]) // 2
    slack = jnp.where((donor == ranking[0]) | (receiver == ranking[0]) | (lengths[receiver] == 0), 0, jnp.maximum(slack, 0))
    shifted = jax.random.randint(jax.random.fold_in(own, 4), (count // 2,), 0, 1 << 20) % (slack + 1)
    lengths = lengths.at[donor].add(-shifted).at[receiver].add(shifted)
    labels = jnp.searchsorted(jnp.cumsum(lengths), jnp.arange(rows * top), side="right").astype(jnp.int32)
    table = labels.reshape(top, rows).T
    table = table[jax.random.permutation(jax.random.fold_in(own, 1), rows)]
    rotation = jax.random.randint(jax.random.fold_in(own, 2), (rows, 1), 0, top)
    return jnp.take_along_axis(table, (jnp.arange(top)[None, :] + rotation) % top, axis=1)


def shares(amount, total, limit, lean, full):
    weights = [(1 << 20) // math.isqrt(standing ** lean) + 1 for standing in range(1, amount + 1)]
    largest = limit if full else min(limit, max(-(-total // amount), total * weights[0] // sum(weights)))
    least = 1 if total - largest >= amount - 1 else 0
    holding, rest = [largest] + [least] * (amount - 1), total - largest - least * (amount - 1)
    while rest > 0:
        movable = [i for i in range(1, amount) if holding[i] < largest] or [i for i in range(1, amount) if holding[i] < limit]
        whole, remaining = sum([weights[i] for i in movable]), rest
        for i in movable:
            more = min(limit - holding[i], max(1, remaining * weights[i] // whole), rest)
            holding[i] = holding[i] + more
            rest = rest - more
    return np.array(holding)


def noise(rng, dims, width, limit, cuts=(), held_as=jnp.bfloat16):
    loudness = shard_levels(rng, dims, cuts, -0.22, 0.18) if cuts else 1.0
    values = jax.random.normal(rng, dims, jnp.float32) * width * loudness
    return jnp.minimum(jnp.maximum(values, -limit), limit).astype(held_as)


def setup_inputs(seed: int = 0) -> dict:
    key_list = jax.random.split(jax.random.key(seed), 8)
    tokens = noise(key_list[0], (TOKENS, D), 1.0, 6.0, ((0, 256),))
    out_grad = noise(key_list[1], (TOKENS, D), 0.125, 0.75, ((0, 256),))
    routes_keys = jax.random.split(jax.random.fold_in(key_list[2], 1), TOKENS // TOK_DEV)
    routes_turns = jax.random.permutation(jax.random.fold_in(key_list[2], 3), TOKENS // TOK_DEV)
    routes = jax.vmap(lambda own, number: routed_block(jax.random.fold_in(key_list[2], 2), own, number, TOK_DEV, EXPERTS, TOP, CAP, 2))(routes_keys, routes_turns).reshape((TOKENS, TOP))
    gate_probs = jnp.clip(0.049804688 + 0.9501953 * jax.random.uniform(key_list[3], (TOKENS, TOP), jnp.float32) ** shard_levels(key_list[3], (TOKENS, TOP), ((0, 256),), -0.2, 0.2), 0.049804688, 1.0).astype(jnp.bfloat16)
    w_gate = noise(key_list[4], (EXPERTS, D, H), D ** -0.5, 0.09375, ((0, 64), (2, 4)))
    w_up = noise(key_list[5], (EXPERTS, D, H), D ** -0.5, 0.09375, ((0, 64), (2, 4)))
    w_down = noise(key_list[6], (EXPERTS, H, D), H ** -0.5, 0.21875, ((0, 64), (1, 4)))
    return dict(tokens=tokens, out_grad=out_grad, routes=routes, gate_probs=gate_probs, w_gate=w_gate, w_up=w_up, w_down=w_down)


def expert_grads(pieces):
    rows_in, rows_dy, rows_prob, gate_w, up_w, down_w = pieces
    gate_pre = jnp.dot(rows_in, gate_w, preferred_element_type=jnp.float32)
    up_pre = jnp.dot(rows_in, up_w, preferred_element_type=jnp.float32)
    sigmoid_gate = jax.nn.sigmoid(gate_pre)
    active = gate_pre * sigmoid_gate
    hidden = (active * up_pre).astype(jnp.bfloat16)
    back_raw = jnp.dot(rows_dy, down_w.T, preferred_element_type=jnp.float32)
    scores = jnp.sum(back_raw * hidden.astype(jnp.float32), axis=1)
    weight_col = rows_prob.astype(jnp.float32)[:, None]
    scaled = (weight_col * rows_dy.astype(jnp.float32)).astype(jnp.bfloat16)
    grad_down = jnp.dot(hidden.T, scaled, preferred_element_type=jnp.float32).astype(jnp.bfloat16)
    back_hidden = weight_col * back_raw
    grad_gate_pre = (back_hidden * up_pre * sigmoid_gate * (1.0 + gate_pre * (1.0 - sigmoid_gate))).astype(jnp.bfloat16)
    grad_up_pre = (back_hidden * active).astype(jnp.bfloat16)
    grad_gate = jnp.dot(rows_in.T, grad_gate_pre, preferred_element_type=jnp.float32).astype(jnp.bfloat16)
    grad_up = jnp.dot(rows_in.T, grad_up_pre, preferred_element_type=jnp.float32).astype(jnp.bfloat16)
    block_width = H // N_DP
    summed = jnp.zeros((rows_in.shape[0], D), jnp.float32)
    for quarter in range(N_DP):
        start_col = quarter * block_width
        stop_col = start_col + block_width
        block_sum = jnp.dot(grad_gate_pre[:, start_col:stop_col], gate_w[:, start_col:stop_col].T, preferred_element_type=jnp.float32)
        block_sum = block_sum + jnp.dot(grad_up_pre[:, start_col:stop_col], up_w[:, start_col:stop_col].T, preferred_element_type=jnp.float32)
        rounded = lax.optimization_barrier(block_sum.astype(jnp.bfloat16))
        summed = summed + rounded.astype(jnp.float32)
    return summed.astype(jnp.bfloat16), scores.astype(jnp.bfloat16), grad_gate, grad_up, grad_down


def reference(tokens, out_grad, routes, gate_probs, w_gate, w_up, w_down):
    one_hot = (routes[:, :, None] == jnp.arange(EXPERTS, dtype=jnp.int32)[None, None, :]).astype(jnp.int32)
    blocked = one_hot.reshape(TOKENS // TOK_DEV, TOK_DEV * TOP, EXPERTS)
    earlier = jnp.cumsum(blocked, axis=1) - blocked
    slot_index = jnp.sum(earlier * blocked, axis=2).reshape(TOKENS, TOP).astype(jnp.int32)
    block_index = (jnp.arange(TOKENS, dtype=jnp.int32) // TOK_DEV)[:, None]
    row_index = (block_index * CAP + slot_index).astype(jnp.int32)
    row_count = (TOKENS // TOK_DEV) * CAP
    spread_in = jnp.broadcast_to(tokens[:, None, :], (TOKENS, TOP, D))
    spread_dy = jnp.broadcast_to(out_grad[:, None, :], (TOKENS, TOP, D))
    rows_in = jnp.zeros((EXPERTS, row_count, D), jnp.bfloat16).at[routes, row_index].set(spread_in)
    rows_dy = jnp.zeros((EXPERTS, row_count, D), jnp.bfloat16).at[routes, row_index].set(spread_dy)
    rows_prob = jnp.zeros((EXPERTS, row_count), jnp.bfloat16).at[routes, row_index].set(gate_probs)
    grad_rows, scores, grad_gate, grad_up, grad_down = lax.map(expert_grads, (rows_in, rows_dy, rows_prob, w_gate, w_up, w_down))
    picked = grad_rows[routes, row_index]
    grad_tokens = jnp.sum(picked.astype(jnp.float32), axis=1).astype(jnp.bfloat16)
    grad_probs = scores[routes, row_index]
    return grad_tokens, grad_probs, grad_gate, grad_up, grad_down
```

```python
import jax
import jax.numpy as jnp
from jax import lax
from jax.sharding import PartitionSpec as P

LANES = 128


def body(tokens, out_grad, routes, gate_probs, w_gate, w_up, w_down):
    expert_count = lax.axis_size("expert")
    tok_count, width = tokens.shape
    top_count = routes.shape[1]
    capacity = 3 * tok_count * top_count // (2 * expert_count)
    slot_total = expert_count * capacity
    per_peer = capacity * width // LANES
    flat_routes = routes.reshape(-1)
    one_hot = (flat_routes[:, None] == jnp.arange(expert_count, dtype=jnp.int32)[None, :]).astype(
        jnp.int32
    )
    earlier = jnp.cumsum(one_hot, axis=0) - one_hot
    slot_index = jnp.sum(earlier * one_hot, axis=1)
    destination = flat_routes * capacity + slot_index
    placing = (jnp.arange(slot_total, dtype=jnp.int32)[:, None] == destination[None, :]).astype(
        jnp.bfloat16
    )
    collect = jnp.sum(placing.reshape(slot_total, tok_count, top_count), axis=2)
    sent_in = (
        jnp.dot(collect, tokens, preferred_element_type=jnp.float32)
        .astype(jnp.bfloat16)
        .reshape(expert_count, per_peer, LANES)
    )
    sent_dy = (
        jnp.dot(collect, out_grad, preferred_element_type=jnp.float32)
        .astype(jnp.bfloat16)
        .reshape(expert_count, per_peer, LANES)
    )
    sent_prob = (
        jnp.dot(placing, gate_probs.reshape(-1), preferred_element_type=jnp.float32)
        .astype(jnp.bfloat16)
        .reshape(expert_count, capacity)
    )
    recv_in = lax.all_to_all(sent_in, "expert", 0, 0, tiled=True).reshape(slot_total, width)
    recv_dy = lax.all_to_all(sent_dy, "expert", 0, 0, tiled=True).reshape(slot_total, width)
    recv_prob = lax.all_to_all(sent_prob, "expert", 0, 0, tiled=True).reshape(slot_total)
    dy_ext = jnp.concatenate(
        [recv_dy, jnp.broadcast_to(recv_prob[:, None], (slot_total, LANES))], axis=1
    )
    rows_in = lax.all_gather(recv_in, "dp", axis=0, tiled=True)
    rows_dy_ext = lax.all_gather(dy_ext, "dp", axis=0, tiled=True)
    rows_dy = rows_dy_ext[:, :width]
    rows_prob = rows_dy_ext[:, width]
    gate_w = w_gate[0]
    up_w = w_up[0]
    down_w = w_down[0]
    contract_last = (((1,), (1,)), ((), ()))
    contract_first = (((0,), (0,)), ((), ()))
    gate_pre = jnp.dot(rows_in, gate_w, preferred_element_type=jnp.float32)
    up_pre = jnp.dot(rows_in, up_w, preferred_element_type=jnp.float32)
    sigmoid_gate = jax.nn.sigmoid(gate_pre)
    active = gate_pre * sigmoid_gate
    hidden = (active * up_pre).astype(jnp.bfloat16)
    back_raw = lax.dot_general(rows_dy, down_w, contract_last, preferred_element_type=jnp.float32)
    score_part = jnp.sum(back_raw * hidden.astype(jnp.float32), axis=1)
    weight_col = rows_prob.astype(jnp.float32)[:, None]
    scaled = (weight_col * rows_dy.astype(jnp.float32)).astype(jnp.bfloat16)
    back_hidden = weight_col * back_raw
    grad_gate_pre = (
        back_hidden * up_pre * sigmoid_gate * (1.0 + gate_pre * (1.0 - sigmoid_gate))
    ).astype(jnp.bfloat16)
    grad_up_pre = (back_hidden * active).astype(jnp.bfloat16)
    row_part = lax.dot_general(
        grad_gate_pre, gate_w, contract_last, preferred_element_type=jnp.float32
    )
    row_part = row_part + lax.dot_general(
        grad_up_pre, up_w, contract_last, preferred_element_type=jnp.float32
    )
    row_total = row_part.shape[0]
    row_ext = jnp.concatenate(
        [row_part, jnp.broadcast_to(score_part[:, None], (row_total, LANES))], axis=1
    ).astype(jnp.bfloat16)
    own_ext = lax.psum_scatter(row_ext, "dp", scatter_dimension=0, tiled=True)
    grad_down = lax.dot_general(
        hidden, scaled, contract_first, preferred_element_type=jnp.float32
    ).astype(jnp.bfloat16)
    grad_gate = lax.dot_general(
        rows_in, grad_gate_pre, contract_first, preferred_element_type=jnp.float32
    ).astype(jnp.bfloat16)
    grad_up = lax.dot_general(
        rows_in, grad_up_pre, contract_first, preferred_element_type=jnp.float32
    ).astype(jnp.bfloat16)
    own_rows = own_ext[:, :width].reshape(expert_count, per_peer, LANES)
    own_scores = own_ext[:, width].reshape(expert_count, capacity)
    back_rows = lax.all_to_all(own_rows, "expert", 0, 0, tiled=True).reshape(slot_total, width)
    back_scores = lax.all_to_all(own_scores, "expert", 0, 0, tiled=True).reshape(slot_total)
    grad_tokens = lax.dot_general(
        collect, back_rows, contract_first, preferred_element_type=jnp.float32
    ).astype(jnp.bfloat16)
    grad_probs = (
        jnp.dot(back_scores, placing, preferred_element_type=jnp.float32)
        .astype(jnp.bfloat16)
        .reshape(tok_count, top_count)
    )
    return (grad_tokens, grad_probs, grad_gate[None], grad_up[None], grad_down[None])


def solution(mesh):
    in_specs = (
        P(("dp", "expert"), None),
        P(("dp", "expert"), None),
        P(("dp", "expert"), None),
        P(("dp", "expert"), None),
        P("expert", None, "dp"),
        P("expert", None, "dp"),
        P("expert", "dp", None),
    )
    out_specs = (
        P(("dp", "expert"), None),
        P(("dp", "expert"), None),
        P("expert", None, "dp"),
        P("expert", None, "dp"),
        P("expert", "dp", None),
    )
    return jax.shard_map(body, mesh=mesh, in_specs=in_specs, out_specs=out_specs, check_vma=False)
```

```python
import jax
import jax.numpy as jnp
from jax import lax
from jax.sharding import PartitionSpec as P

LANES = 128
CHUNKS = 2


def body(tokens, out_grad, routes, gate_probs, w_gate, w_up, w_down):
    expert_count = lax.axis_size("expert")
    tok_count, width = tokens.shape
    top_count = routes.shape[1]
    capacity = 3 * tok_count * top_count // (2 * expert_count)
    slot_total = expert_count * capacity
    piece = width // CHUNKS
    per_peer = capacity * piece // LANES
    flat_routes = routes.reshape(-1)
    one_hot = (flat_routes[:, None] == jnp.arange(expert_count, dtype=jnp.int32)[None, :]).astype(
        jnp.int32
    )
    earlier = jnp.cumsum(one_hot, axis=0) - one_hot
    slot_index = jnp.sum(earlier * one_hot, axis=1)
    destination = flat_routes * capacity + slot_index
    placing = (jnp.arange(slot_total, dtype=jnp.int32)[:, None] == destination[None, :]).astype(
        jnp.bfloat16
    )
    collect = jnp.sum(placing.reshape(slot_total, tok_count, top_count), axis=2)
    contract_last = (((1,), (1,)), ((), ()))
    contract_first = (((0,), (0,)), ((), ()))

    def to_expert(rows):
        shaped = rows.reshape(expert_count, per_peer, LANES)
        return lax.all_to_all(shaped, "expert", 0, 0, tiled=True).reshape(slot_total, piece)

    def dispatch(source, c):
        part = source[:, c * piece:(c + 1) * piece]
        rows = jnp.dot(collect, part, preferred_element_type=jnp.float32).astype(jnp.bfloat16)
        return to_expert(rows)

    sent_prob = (
        jnp.dot(placing, gate_probs.reshape(-1), preferred_element_type=jnp.float32)
        .astype(jnp.bfloat16)
        .reshape(expert_count, capacity)
    )
    recv_prob = lax.all_to_all(sent_prob, "expert", 0, 0, tiled=True).reshape(slot_total)
    rows_in = []
    for c in range(CHUNKS):
        rows_in.append(lax.all_gather(dispatch(tokens, c), "dp", axis=0, tiled=True))
    rows_dy = []
    rows_prob = None
    for c in range(CHUNKS):
        recv = dispatch(out_grad, c)
        if c == 0:
            recv = jnp.concatenate(
                [recv, jnp.broadcast_to(recv_prob[:, None], (slot_total, LANES))], axis=1
            )
        gathered = lax.all_gather(recv, "dp", axis=0, tiled=True)
        if c == 0:
            rows_prob = gathered[:, piece]
            gathered = gathered[:, :piece]
        rows_dy.append(gathered)
    gate_w = w_gate[0]
    up_w = w_up[0]
    down_w = w_down[0]
    gate_pre = None
    up_pre = None
    for c in range(CHUNKS):
        g = jnp.dot(rows_in[c], gate_w[c * piece:(c + 1) * piece], preferred_element_type=jnp.float32)
        u = jnp.dot(rows_in[c], up_w[c * piece:(c + 1) * piece], preferred_element_type=jnp.float32)
        gate_pre = g if gate_pre is None else gate_pre + g
        up_pre = u if up_pre is None else up_pre + u
    sigmoid_gate = jax.nn.sigmoid(gate_pre)
    active = gate_pre * sigmoid_gate
    hidden = (active * up_pre).astype(jnp.bfloat16)
    back_raw = None
    for c in range(CHUNKS):
        b = lax.dot_general(
            rows_dy[c], down_w[:, c * piece:(c + 1) * piece], contract_last,
            preferred_element_type=jnp.float32,
        )
        back_raw = b if back_raw is None else back_raw + b
    score_part = jnp.sum(back_raw * hidden.astype(jnp.float32), axis=1)
    weight_col = rows_prob.astype(jnp.float32)[:, None]
    back_hidden = weight_col * back_raw
    grad_gate_pre = (
        back_hidden * up_pre * sigmoid_gate * (1.0 + gate_pre * (1.0 - sigmoid_gate))
    ).astype(jnp.bfloat16)
    grad_up_pre = (back_hidden * active).astype(jnp.bfloat16)
    row_total = grad_gate_pre.shape[0]
    back_rows = []
    back_scores = None
    for c in range(CHUNKS):
        part = lax.dot_general(
            grad_gate_pre, gate_w[c * piece:(c + 1) * piece], contract_last,
            preferred_element_type=jnp.float32,
        )
        part = part + lax.dot_general(
            grad_up_pre, up_w[c * piece:(c + 1) * piece], contract_last,
            preferred_element_type=jnp.float32,
        )
        if c == 0:
            part = jnp.concatenate(
                [part, jnp.broadcast_to(score_part[:, None], (row_total, LANES))], axis=1
            )
        own = lax.psum_scatter(part.astype(jnp.bfloat16), "dp", scatter_dimension=0, tiled=True)
        if c == 0:
            own_scores = own[:, piece].reshape(expert_count, capacity)
            back_scores = lax.all_to_all(own_scores, "expert", 0, 0, tiled=True).reshape(slot_total)
            own = own[:, :piece]
        back_rows.append(to_expert(own))
    grad_down = []
    grad_gate = []
    grad_up = []
    for c in range(CHUNKS):
        dy_c = rows_dy[c]
        scaled = (weight_col * dy_c.astype(jnp.float32)).astype(jnp.bfloat16)
        grad_down.append(lax.dot_general(
            hidden, scaled, contract_first, preferred_element_type=jnp.float32
        ).astype(jnp.bfloat16))
        grad_gate.append(lax.dot_general(
            rows_in[c], grad_gate_pre, contract_first, preferred_element_type=jnp.float32
        ).astype(jnp.bfloat16))
        grad_up.append(lax.dot_general(
            rows_in[c], grad_up_pre, contract_first, preferred_element_type=jnp.float32
        ).astype(jnp.bfloat16))
    grad_down = jnp.concatenate(grad_down, axis=1)
    grad_gate = jnp.concatenate(grad_gate, axis=0)
    grad_up = jnp.concatenate(grad_up, axis=0)
    grad_tokens = jnp.concatenate(
        [
            lax.dot_general(
                collect, back_rows[c], contract_first, preferred_element_type=jnp.float32
            ).astype(jnp.bfloat16)
            for c in range(CHUNKS)
        ],
        axis=1,
    )
    grad_probs = (
        jnp.dot(back_scores, placing, preferred_element_type=jnp.float32)
        .astype(jnp.bfloat16)
        .reshape(tok_count, top_count)
    )
    return (grad_tokens, grad_probs, grad_gate[None], grad_up[None], grad_down[None])


def solution(mesh):
    in_specs = (
        P(("dp", "expert"), None),
        P(("dp", "expert"), None),
        P(("dp", "expert"), None),
        P(("dp", "expert"), None),
        P("expert", None, "dp"),
        P("expert", None, "dp"),
        P("expert", "dp", None),
    )
    out_specs = (
        P(("dp", "expert"), None),
        P(("dp", "expert"), None),
        P("expert", None, "dp"),
        P("expert", None, "dp"),
        P("expert", "dp", None),
    )
    return jax.shard_map(body, mesh=mesh, in_specs=in_specs, out_specs=out_specs, check_vma=False)
```

```python
import jax
import jax.numpy as jnp
from jax import lax
from jax.sharding import PartitionSpec as P

LANES = 128


def ring_pairs(count, step):
    return [(i, (i + step) % count) for i in range(count)]


def ring_gather(x, axis):
    count = lax.axis_size(axis)
    fwd = ring_pairs(count, 1)
    bwd = ring_pairs(count, -1)
    half = x.shape[0] // 2
    from_prev = lax.ppermute(x, axis, fwd)
    from_next = lax.ppermute(x, axis, bwd)
    far_a = lax.ppermute(from_prev[:half], axis, fwd)
    far_b = lax.ppermute(from_next[half:], axis, bwd)
    return jnp.concatenate([x, from_next, far_a, far_b, from_prev], axis=0)


def ring_reduce_scatter(parts, axis):
    count = lax.axis_size(axis)
    fwd = ring_pairs(count, 1)
    bwd = ring_pairs(count, -1)
    block = parts.shape[0] // count
    half = block // 2
    own, to_next, far, to_prev = (parts[k * block:(k + 1) * block] for k in range(count))
    got_a = lax.ppermute(far[:half].astype(jnp.bfloat16), axis, fwd).astype(jnp.float32)
    got_b = lax.ppermute(far[half:].astype(jnp.bfloat16), axis, bwd).astype(jnp.float32)
    send_next = jnp.concatenate([to_next[:half] + got_a, to_next[half:]], axis=0)
    send_prev = jnp.concatenate([to_prev[:half], to_prev[half:] + got_b], axis=0)
    from_prev = lax.ppermute(send_next.astype(jnp.bfloat16), axis, fwd).astype(jnp.float32)
    from_next = lax.ppermute(send_prev.astype(jnp.bfloat16), axis, bwd).astype(jnp.float32)
    return own + from_prev + from_next


def body(tokens, out_grad, routes, gate_probs, w_gate, w_up, w_down):
    expert_count = lax.axis_size("expert")
    tok_count, width = tokens.shape
    top_count = routes.shape[1]
    capacity = 3 * tok_count * top_count // (2 * expert_count)
    slot_total = expert_count * capacity
    per_peer = capacity * width // LANES
    flat_routes = routes.reshape(-1)
    one_hot = (flat_routes[:, None] == jnp.arange(expert_count, dtype=jnp.int32)[None, :]).astype(
        jnp.int32
    )
    earlier = jnp.cumsum(one_hot, axis=0) - one_hot
    slot_index = jnp.sum(earlier * one_hot, axis=1)
    destination = flat_routes * capacity + slot_index
    placing = (jnp.arange(slot_total, dtype=jnp.int32)[:, None] == destination[None, :]).astype(
        jnp.bfloat16
    )
    collect = jnp.sum(placing.reshape(slot_total, tok_count, top_count), axis=2)
    sent_in = (
        jnp.dot(collect, tokens, preferred_element_type=jnp.float32)
        .astype(jnp.bfloat16)
        .reshape(expert_count, per_peer, LANES)
    )
    sent_dy = (
        jnp.dot(collect, out_grad, preferred_element_type=jnp.float32)
        .astype(jnp.bfloat16)
        .reshape(expert_count, per_peer, LANES)
    )
    sent_prob = (
        jnp.dot(placing, gate_probs.reshape(-1), preferred_element_type=jnp.float32)
        .astype(jnp.bfloat16)
        .reshape(expert_count, capacity)
    )
    recv_in = lax.all_to_all(sent_in, "expert", 0, 0, tiled=True).reshape(slot_total, width)
    recv_dy = lax.all_to_all(sent_dy, "expert", 0, 0, tiled=True).reshape(slot_total, width)
    recv_prob = lax.all_to_all(sent_prob, "expert", 0, 0, tiled=True).reshape(slot_total)
    dy_ext = jnp.concatenate(
        [recv_dy, jnp.broadcast_to(recv_prob[:, None], (slot_total, LANES))], axis=1
    )
    rows_in = ring_gather(recv_in, "dp")
    rows_dy_ext = ring_gather(dy_ext, "dp")
    rows_dy = rows_dy_ext[:, :width]
    rows_prob = rows_dy_ext[:, width]
    gate_w = w_gate[0]
    up_w = w_up[0]
    down_w = w_down[0]
    contract_last = (((1,), (1,)), ((), ()))
    contract_first = (((0,), (0,)), ((), ()))
    gate_pre = jnp.dot(rows_in, gate_w, preferred_element_type=jnp.float32)
    up_pre = jnp.dot(rows_in, up_w, preferred_element_type=jnp.float32)
    sigmoid_gate = jax.nn.sigmoid(gate_pre)
    active = gate_pre * sigmoid_gate
    hidden = (active * up_pre).astype(jnp.bfloat16)
    back_raw = lax.dot_general(rows_dy, down_w, contract_last, preferred_element_type=jnp.float32)
    score_part = jnp.sum(back_raw * hidden.astype(jnp.float32), axis=1)
    weight_col = rows_prob.astype(jnp.float32)[:, None]
    scaled = (weight_col * rows_dy.astype(jnp.float32)).astype(jnp.bfloat16)
    back_hidden = weight_col * back_raw
    grad_gate_pre = (
        back_hidden * up_pre * sigmoid_gate * (1.0 + gate_pre * (1.0 - sigmoid_gate))
    ).astype(jnp.bfloat16)
    grad_up_pre = (back_hidden * active).astype(jnp.bfloat16)
    row_part = lax.dot_general(
        grad_gate_pre, gate_w, contract_last, preferred_element_type=jnp.float32
    )
    row_part = row_part + lax.dot_general(
        grad_up_pre, up_w, contract_last, preferred_element_type=jnp.float32
    )
    row_total = row_part.shape[0]
    row_ext = jnp.concatenate(
        [row_part, jnp.broadcast_to(score_part[:, None], (row_total, LANES))], axis=1
    )
    own_ext = ring_reduce_scatter(row_ext, "dp").astype(jnp.bfloat16)
    grad_down = lax.dot_general(
        hidden, scaled, contract_first, preferred_element_type=jnp.float32
    ).astype(jnp.bfloat16)
    grad_gate = lax.dot_general(
        rows_in, grad_gate_pre, contract_first, preferred_element_type=jnp.float32
    ).astype(jnp.bfloat16)
    grad_up = lax.dot_general(
        rows_in, grad_up_pre, contract_first, preferred_element_type=jnp.float32
    ).astype(jnp.bfloat16)
    own_rows = own_ext[:, :width].reshape(expert_count, per_peer, LANES)
    own_scores = own_ext[:, width].reshape(expert_count, capacity)
    back_rows = lax.all_to_all(own_rows, "expert", 0, 0, tiled=True).reshape(slot_total, width)
    back_scores = lax.all_to_all(own_scores, "expert", 0, 0, tiled=True).reshape(slot_total)
    grad_tokens = lax.dot_general(
        collect, back_rows, contract_first, preferred_element_type=jnp.float32
    ).astype(jnp.bfloat16)
    grad_probs = (
        jnp.dot(back_scores, placing, preferred_element_type=jnp.float32)
        .astype(jnp.bfloat16)
        .reshape(tok_count, top_count)
    )
    return (grad_tokens, grad_probs, grad_gate[None], grad_up[None], grad_down[None])


def solution(mesh):
    in_specs = (
        P(("dp", "expert"), None),
        P(("dp", "expert"), None),
        P(("dp", "expert"), None),
        P(("dp", "expert"), None),
        P("expert", None, "dp"),
        P("expert", None, "dp"),
        P("expert", "dp", None),
    )
    out_specs = (
        P(("dp", "expert"), None),
        P(("dp", "expert"), None),
        P("expert", None, "dp"),
        P("expert", None, "dp"),
        P("expert", "dp", None),
    )
    return jax.shard_map(body, mesh=mesh, in_specs=in_specs, out_specs=out_specs, check_vma=False)
```

```python
import jax
import jax.numpy as jnp
from jax import lax
from jax.sharding import PartitionSpec as P

LANES = 128


def ring_pairs(count, step):
    return [(i, (i + step) % count) for i in range(count)]


def ring_gather(x, axis):
    count = lax.axis_size(axis)
    fwd = ring_pairs(count, 1)
    bwd = ring_pairs(count, -1)
    half = x.shape[0] // 2
    from_prev = lax.ppermute(x, axis, fwd)
    from_next = lax.ppermute(x, axis, bwd)
    far_a = lax.ppermute(from_prev[:half], axis, fwd)
    far_b = lax.ppermute(from_next[half:], axis, bwd)
    return jnp.concatenate([x, from_next, far_a, far_b, from_prev], axis=0)


def ring_reduce_scatter(parts, axis):
    count = lax.axis_size(axis)
    fwd = ring_pairs(count, 1)
    bwd = ring_pairs(count, -1)
    block = parts.shape[0] // count
    half = block // 2
    own, to_next, far, to_prev = (parts[k * block:(k + 1) * block] for k in range(count))
    got_a = lax.ppermute(far[:half].astype(jnp.bfloat16), axis, fwd).astype(jnp.float32)
    got_b = lax.ppermute(far[half:].astype(jnp.bfloat16), axis, bwd).astype(jnp.float32)
    send_next = jnp.concatenate([to_next[:half] + got_a, to_next[half:]], axis=0)
    send_prev = jnp.concatenate([to_prev[:half], to_prev[half:] + got_b], axis=0)
    from_prev = lax.ppermute(send_next.astype(jnp.bfloat16), axis, fwd).astype(jnp.float32)
    from_next = lax.ppermute(send_prev.astype(jnp.bfloat16), axis, bwd).astype(jnp.float32)
    return own + from_prev + from_next


def body(tokens, out_grad, routes, gate_probs, w_gate, w_up, w_down):
    expert_count = lax.axis_size("expert")
    tok_count, width = tokens.shape
    top_count = routes.shape[1]
    capacity = 3 * tok_count * top_count // (2 * expert_count)
    slot_total = expert_count * capacity
    per_peer = capacity * width // LANES
    flat_routes = routes.reshape(-1)
    one_hot = (flat_routes[:, None] == jnp.arange(expert_count, dtype=jnp.int32)[None, :]).astype(
        jnp.int32
    )
    earlier = jnp.cumsum(one_hot, axis=0) - one_hot
    slot_index = jnp.sum(earlier * one_hot, axis=1)
    destination = flat_routes * capacity + slot_index
    placing = (jnp.arange(slot_total, dtype=jnp.int32)[:, None] == destination[None, :]).astype(
        jnp.bfloat16
    )
    collect = jnp.sum(placing.reshape(slot_total, tok_count, top_count), axis=2)
    sent_in = (
        jnp.dot(collect, tokens, preferred_element_type=jnp.float32)
        .astype(jnp.bfloat16)
        .reshape(expert_count, per_peer, LANES)
    )
    weighted = jnp.sum(
        placing.reshape(slot_total, tok_count, top_count) * gate_probs[None, :, :], axis=2
    )
    sent_dy = (
        jnp.dot(weighted, out_grad, preferred_element_type=jnp.float32)
        .astype(jnp.bfloat16)
        .reshape(expert_count, per_peer, LANES)
    )
    recv_in = lax.all_to_all(sent_in, "expert", 0, 0, tiled=True).reshape(slot_total, width)
    recv_dy = lax.all_to_all(sent_dy, "expert", 0, 0, tiled=True).reshape(slot_total, width)
    rows_in = ring_gather(recv_in, "dp")
    rows_dy = ring_gather(recv_dy, "dp")
    gate_w = w_gate[0]
    up_w = w_up[0]
    down_w = w_down[0]
    contract_last = (((1,), (1,)), ((), ()))
    contract_first = (((0,), (0,)), ((), ()))
    gate_pre = jnp.dot(rows_in, gate_w, preferred_element_type=jnp.float32)
    up_pre = jnp.dot(rows_in, up_w, preferred_element_type=jnp.float32)
    sigmoid_gate = jax.nn.sigmoid(gate_pre)
    active = gate_pre * sigmoid_gate
    hidden = (active * up_pre).astype(jnp.bfloat16)
    back_hidden = lax.dot_general(
        rows_dy, down_w, contract_last, preferred_element_type=jnp.float32
    )
    score_part = jnp.sum(back_hidden * hidden.astype(jnp.float32), axis=1)
    scaled = rows_dy
    grad_gate_pre = (
        back_hidden * up_pre * sigmoid_gate * (1.0 + gate_pre * (1.0 - sigmoid_gate))
    ).astype(jnp.bfloat16)
    grad_up_pre = (back_hidden * active).astype(jnp.bfloat16)
    row_part = lax.dot_general(
        grad_gate_pre, gate_w, contract_last, preferred_element_type=jnp.float32
    )
    row_part = row_part + lax.dot_general(
        grad_up_pre, up_w, contract_last, preferred_element_type=jnp.float32
    )
    row_total = row_part.shape[0]
    row_ext = jnp.concatenate(
        [row_part, jnp.broadcast_to(score_part[:, None], (row_total, LANES))], axis=1
    )
    own_ext = ring_reduce_scatter(row_ext, "dp").astype(jnp.bfloat16)
    grad_down = lax.dot_general(
        hidden, scaled, contract_first, preferred_element_type=jnp.float32
    ).astype(jnp.bfloat16)
    grad_gate = lax.dot_general(
        rows_in, grad_gate_pre, contract_first, preferred_element_type=jnp.float32
    ).astype(jnp.bfloat16)
    grad_up = lax.dot_general(
        rows_in, grad_up_pre, contract_first, preferred_element_type=jnp.float32
    ).astype(jnp.bfloat16)
    own_rows = own_ext[:, :width].reshape(expert_count, per_peer, LANES)
    own_scores = own_ext[:, width].reshape(expert_count, 1, capacity)
    score_tile = jnp.pad(own_scores, ((0, 0), (0, 15), (0, LANES - capacity)))
    back_ext = lax.all_to_all(
        jnp.concatenate([own_rows, score_tile], axis=1), "expert", 0, 0, tiled=True
    )
    back_rows = back_ext[:, :per_peer].reshape(slot_total, width)
    back_scores = back_ext[:, per_peer, :capacity].reshape(slot_total)
    grad_tokens = lax.dot_general(
        collect, back_rows, contract_first, preferred_element_type=jnp.float32
    ).astype(jnp.bfloat16)
    weighted_scores = jnp.dot(back_scores, placing, preferred_element_type=jnp.float32)
    grad_probs = (
        (weighted_scores / gate_probs.reshape(-1).astype(jnp.float32))
        .astype(jnp.bfloat16)
        .reshape(tok_count, top_count)
    )
    return (grad_tokens, grad_probs, grad_gate[None], grad_up[None], grad_down[None])


def solution(mesh):
    in_specs = (
        P(("dp", "expert"), None),
        P(("dp", "expert"), None),
        P(("dp", "expert"), None),
        P(("dp", "expert"), None),
        P("expert", None, "dp"),
        P("expert", None, "dp"),
        P("expert", "dp", None),
    )
    out_specs = (
        P(("dp", "expert"), None),
        P(("dp", "expert"), None),
        P("expert", None, "dp"),
        P("expert", None, "dp"),
        P("expert", "dp", None),
    )
    return jax.shard_map(body, mesh=mesh, in_specs=in_specs, out_specs=out_specs, check_vma=False)
```

```python
import jax
import jax.numpy as jnp
from jax import lax
from jax.sharding import PartitionSpec as P

LANES = 128


def ring_pairs(count, step):
    return [(i, (i + step) % count) for i in range(count)]


def ring_gather(x, axis):
    count = lax.axis_size(axis)
    fwd = ring_pairs(count, 1)
    bwd = ring_pairs(count, -1)
    half = x.shape[0] // 2
    from_prev = lax.ppermute(x, axis, fwd)
    from_next = lax.ppermute(x, axis, bwd)
    far_a = lax.ppermute(from_prev[:half], axis, fwd)
    far_b = lax.ppermute(from_next[half:], axis, bwd)
    return jnp.concatenate([x, from_next, far_a, far_b, from_prev], axis=0)


def ring_reduce_scatter(blocks, axis, wire):
    count = lax.axis_size(axis)
    fwd = ring_pairs(count, 1)
    bwd = ring_pairs(count, -1)
    own, to_next, far, to_prev = blocks
    half = own.shape[0] // 2
    got_a = lax.ppermute(far[:half].astype(wire), axis, fwd).astype(jnp.float32)
    got_b = lax.ppermute(far[half:].astype(wire), axis, bwd).astype(jnp.float32)
    send_next = jnp.concatenate([to_next[:half] + got_a, to_next[half:]], axis=0)
    send_prev = jnp.concatenate([to_prev[:half], to_prev[half:] + got_b], axis=0)
    from_prev = lax.ppermute(send_next.astype(wire), axis, fwd).astype(jnp.float32)
    from_next = lax.ppermute(send_prev.astype(wire), axis, bwd).astype(jnp.float32)
    return own + from_prev + from_next


def body(tokens, out_grad, routes, gate_probs, w_gate, w_up, w_down):
    expert_count = lax.axis_size("expert")
    tok_count, width = tokens.shape
    top_count = routes.shape[1]
    capacity = 3 * tok_count * top_count // (2 * expert_count)
    slot_total = expert_count * capacity
    per_peer = capacity * width // LANES
    flat_routes = routes.reshape(-1)
    one_hot = (flat_routes[:, None] == jnp.arange(expert_count, dtype=jnp.int32)[None, :]).astype(
        jnp.int32
    )
    earlier = jnp.cumsum(one_hot, axis=0) - one_hot
    slot_index = jnp.sum(earlier * one_hot, axis=1)
    destination = flat_routes * capacity + slot_index
    placing = (jnp.arange(slot_total, dtype=jnp.int32)[:, None] == destination[None, :]).astype(
        jnp.bfloat16
    )
    collect = jnp.sum(placing.reshape(slot_total, tok_count, top_count), axis=2)
    sent_in = (
        jnp.dot(collect, tokens, preferred_element_type=jnp.float32)
        .astype(jnp.bfloat16)
        .reshape(expert_count, per_peer, LANES)
    )
    weighted = jnp.sum(
        placing.reshape(slot_total, tok_count, top_count) * gate_probs[None, :, :], axis=2
    )
    sent_dy = (
        jnp.dot(weighted, out_grad, preferred_element_type=jnp.float32)
        .astype(jnp.bfloat16)
        .reshape(expert_count, per_peer, LANES)
    )
    recv_in = lax.all_to_all(sent_in, "expert", 0, 0, tiled=True).reshape(slot_total, width)
    recv_dy = lax.all_to_all(sent_dy, "expert", 0, 0, tiled=True).reshape(slot_total, width)
    rows_in = ring_gather(recv_in, "dp")
    rows_dy = ring_gather(recv_dy, "dp")
    gate_w = w_gate[0]
    up_w = w_up[0]
    down_w = w_down[0]
    contract_last = (((1,), (1,)), ((), ()))
    contract_first = (((0,), (0,)), ((), ()))
    gate_pre = jnp.dot(rows_in, gate_w, preferred_element_type=jnp.float32)
    up_pre = jnp.dot(rows_in, up_w, preferred_element_type=jnp.float32)
    sigmoid_gate = jax.nn.sigmoid(gate_pre)
    active = gate_pre * sigmoid_gate
    hidden = (active * up_pre).astype(jnp.bfloat16)
    back_hidden = lax.dot_general(
        rows_dy, down_w, contract_last, preferred_element_type=jnp.float32
    )
    score_part = jnp.sum(back_hidden * hidden.astype(jnp.float32), axis=1)
    scaled = rows_dy
    grad_gate_pre = (
        back_hidden * up_pre * sigmoid_gate * (1.0 + gate_pre * (1.0 - sigmoid_gate))
    ).astype(jnp.bfloat16)
    grad_up_pre = (back_hidden * active).astype(jnp.bfloat16)
    row_total = grad_gate_pre.shape[0]
    dp_count = lax.axis_size("dp")
    block = row_total // dp_count
    row_blocks = []
    for k in range(dp_count):
        rows = slice(k * block, (k + 1) * block)
        part = lax.dot_general(
            grad_gate_pre[rows], gate_w, contract_last, preferred_element_type=jnp.float32
        )
        part = part + lax.dot_general(
            grad_up_pre[rows], up_w, contract_last, preferred_element_type=jnp.float32
        )
        row_blocks.append(part)
    own_grad = ring_reduce_scatter(row_blocks, "dp", jnp.bfloat16).astype(jnp.bfloat16)
    score_blocks = [score_part[k * block:(k + 1) * block, None] for k in range(dp_count)]
    own_score = ring_reduce_scatter(score_blocks, "dp", jnp.float32).astype(jnp.bfloat16)
    grad_down = lax.dot_general(
        hidden, scaled, contract_first, preferred_element_type=jnp.float32
    ).astype(jnp.bfloat16)
    grad_gate = lax.dot_general(
        rows_in, grad_gate_pre, contract_first, preferred_element_type=jnp.float32
    ).astype(jnp.bfloat16)
    grad_up = lax.dot_general(
        rows_in, grad_up_pre, contract_first, preferred_element_type=jnp.float32
    ).astype(jnp.bfloat16)
    own_rows = own_grad.reshape(expert_count, per_peer, LANES)
    own_scores = own_score.reshape(expert_count, 1, capacity)
    score_tile = jnp.pad(own_scores, ((0, 0), (0, 15), (0, LANES - capacity)))
    back_ext = lax.all_to_all(
        jnp.concatenate([own_rows, score_tile], axis=1), "expert", 0, 0, tiled=True
    )
    back_rows = back_ext[:, :per_peer].reshape(slot_total, width)
    back_scores = back_ext[:, per_peer, :capacity].reshape(slot_total)
    grad_tokens = lax.dot_general(
        collect, back_rows, contract_first, preferred_element_type=jnp.float32
    ).astype(jnp.bfloat16)
    weighted_scores = jnp.dot(back_scores, placing, preferred_element_type=jnp.float32)
    grad_probs = (
        (weighted_scores / gate_probs.reshape(-1).astype(jnp.float32))
        .astype(jnp.bfloat16)
        .reshape(tok_count, top_count)
    )
    return (grad_tokens, grad_probs, grad_gate[None], grad_up[None], grad_down[None])


def solution(mesh):
    in_specs = (
        P(("dp", "expert"), None),
        P(("dp", "expert"), None),
        P(("dp", "expert"), None),
        P(("dp", "expert"), None),
        P("expert", None, "dp"),
        P("expert", None, "dp"),
        P("expert", "dp", None),
    )
    out_specs = (
        P(("dp", "expert"), None),
        P(("dp", "expert"), None),
        P("expert", None, "dp"),
        P("expert", None, "dp"),
        P("expert", "dp", None),
    )
    return jax.shard_map(body, mesh=mesh, in_specs=in_specs, out_specs=out_specs, check_vma=False)
```

```python
import jax
import jax.numpy as jnp
from jax import lax
from jax.sharding import PartitionSpec as P

LANES = 128
CHUNKS = 2


def ring_pairs(count, step):
    return [(i, (i + step) % count) for i in range(count)]


def ring_gather(x, axis):
    count = lax.axis_size(axis)
    fwd = ring_pairs(count, 1)
    bwd = ring_pairs(count, -1)
    half = x.shape[0] // 2
    from_prev = lax.ppermute(x, axis, fwd)
    from_next = lax.ppermute(x, axis, bwd)
    far_a = lax.ppermute(from_prev[:half], axis, fwd)
    far_b = lax.ppermute(from_next[half:], axis, bwd)
    return jnp.concatenate([x, from_next, far_a, far_b, from_prev], axis=0)


def ring_reduce_scatter(blocks, axis, wire):
    count = lax.axis_size(axis)
    fwd = ring_pairs(count, 1)
    bwd = ring_pairs(count, -1)
    own, to_next, far, to_prev = blocks
    half = own.shape[0] // 2
    got_a = lax.ppermute(far[:half].astype(wire), axis, fwd).astype(jnp.float32)
    got_b = lax.ppermute(far[half:].astype(wire), axis, bwd).astype(jnp.float32)
    send_next = jnp.concatenate([to_next[:half] + got_a, to_next[half:]], axis=0)
    send_prev = jnp.concatenate([to_prev[:half], to_prev[half:] + got_b], axis=0)
    from_prev = lax.ppermute(send_next.astype(wire), axis, fwd).astype(jnp.float32)
    from_next = lax.ppermute(send_prev.astype(wire), axis, bwd).astype(jnp.float32)
    return own + from_prev + from_next


def body(tokens, out_grad, routes, gate_probs, w_gate, w_up, w_down):
    expert_count = lax.axis_size("expert")
    tok_count, width = tokens.shape
    top_count = routes.shape[1]
    capacity = 3 * tok_count * top_count // (2 * expert_count)
    slot_total = expert_count * capacity
    per_peer = capacity * width // LANES
    flat_routes = routes.reshape(-1)
    one_hot = (flat_routes[:, None] == jnp.arange(expert_count, dtype=jnp.int32)[None, :]).astype(
        jnp.int32
    )
    earlier = jnp.cumsum(one_hot, axis=0) - one_hot
    slot_index = jnp.sum(earlier * one_hot, axis=1)
    destination = flat_routes * capacity + slot_index
    placing = (jnp.arange(slot_total, dtype=jnp.int32)[:, None] == destination[None, :]).astype(
        jnp.bfloat16
    )
    collect = jnp.sum(placing.reshape(slot_total, tok_count, top_count), axis=2)
    sent_in = (
        jnp.dot(collect, tokens, preferred_element_type=jnp.float32)
        .astype(jnp.bfloat16)
        .reshape(expert_count, per_peer, LANES)
    )
    weighted = jnp.sum(
        placing.reshape(slot_total, tok_count, top_count) * gate_probs[None, :, :], axis=2
    )
    sent_dy = (
        jnp.dot(weighted, out_grad, preferred_element_type=jnp.float32)
        .astype(jnp.bfloat16)
        .reshape(expert_count, per_peer, LANES)
    )
    recv_in = lax.all_to_all(sent_in, "expert", 0, 0, tiled=True).reshape(slot_total, width)
    recv_dy = lax.all_to_all(sent_dy, "expert", 0, 0, tiled=True).reshape(slot_total, width)
    rows_in = ring_gather(recv_in, "dp")
    rows_dy = ring_gather(recv_dy, "dp")
    gate_w = w_gate[0]
    up_w = w_up[0]
    down_w = w_down[0]
    contract_last = (((1,), (1,)), ((), ()))
    contract_first = (((0,), (0,)), ((), ()))
    gate_pre = jnp.dot(rows_in, gate_w, preferred_element_type=jnp.float32)
    up_pre = jnp.dot(rows_in, up_w, preferred_element_type=jnp.float32)
    sigmoid_gate = jax.nn.sigmoid(gate_pre)
    active = gate_pre * sigmoid_gate
    hidden = (active * up_pre).astype(jnp.bfloat16)
    back_hidden = lax.dot_general(
        rows_dy, down_w, contract_last, preferred_element_type=jnp.float32
    )
    score_part = jnp.sum(back_hidden * hidden.astype(jnp.float32), axis=1)
    scaled = rows_dy
    grad_gate_pre = (
        back_hidden * up_pre * sigmoid_gate * (1.0 + gate_pre * (1.0 - sigmoid_gate))
    ).astype(jnp.bfloat16)
    grad_up_pre = (back_hidden * active).astype(jnp.bfloat16)
    row_total = grad_gate_pre.shape[0]
    dp_count = lax.axis_size("dp")
    block = row_total // dp_count
    score_blocks = [score_part[k * block:(k + 1) * block, None] for k in range(dp_count)]
    own_score = ring_reduce_scatter(score_blocks, "dp", jnp.float32).astype(jnp.bfloat16)
    own_scores = own_score.reshape(expert_count, 1, capacity)
    piece = width // CHUNKS
    per_piece = capacity * piece // LANES
    back_rows = []
    back_scores = None
    for c in range(CHUNKS):
        cols = slice(c * piece, (c + 1) * piece)
        row_blocks = []
        for k in range(dp_count):
            rows = slice(k * block, (k + 1) * block)
            part = lax.dot_general(
                grad_gate_pre[rows], gate_w[cols], contract_last,
                preferred_element_type=jnp.float32,
            )
            part = part + lax.dot_general(
                grad_up_pre[rows], up_w[cols], contract_last,
                preferred_element_type=jnp.float32,
            )
            row_blocks.append(part)
        own_grad = ring_reduce_scatter(row_blocks, "dp", jnp.bfloat16).astype(jnp.bfloat16)
        own_rows = own_grad.reshape(expert_count, per_piece, LANES)
        if c == 0:
            score_tile = jnp.pad(own_scores, ((0, 0), (0, 15), (0, LANES - capacity)))
            own_rows = jnp.concatenate([own_rows, score_tile], axis=1)
        back = lax.all_to_all(own_rows, "expert", 0, 0, tiled=True)
        if c == 0:
            back_scores = back[:, per_piece, :capacity].reshape(slot_total)
            back = back[:, :per_piece]
        back_rows.append(back.reshape(slot_total, piece))
    grad_down = lax.dot_general(
        hidden, scaled, contract_first, preferred_element_type=jnp.float32
    ).astype(jnp.bfloat16)
    grad_gate = lax.dot_general(
        rows_in, grad_gate_pre, contract_first, preferred_element_type=jnp.float32
    ).astype(jnp.bfloat16)
    grad_up = lax.dot_general(
        rows_in, grad_up_pre, contract_first, preferred_element_type=jnp.float32
    ).astype(jnp.bfloat16)
    grad_tokens = jnp.concatenate(
        [
            lax.dot_general(
                collect, back, contract_first, preferred_element_type=jnp.float32
            ).astype(jnp.bfloat16)
            for back in back_rows
        ],
        axis=1,
    )
    weighted_scores = jnp.dot(back_scores, placing, preferred_element_type=jnp.float32)
    grad_probs = (
        (weighted_scores / gate_probs.reshape(-1).astype(jnp.float32))
        .astype(jnp.bfloat16)
        .reshape(tok_count, top_count)
    )
    return (grad_tokens, grad_probs, grad_gate[None], grad_up[None], grad_down[None])


def solution(mesh):
    in_specs = (
        P(("dp", "expert"), None),
        P(("dp", "expert"), None),
        P(("dp", "expert"), None),
        P(("dp", "expert"), None),
        P("expert", None, "dp"),
        P("expert", None, "dp"),
        P("expert", "dp", None),
    )
    out_specs = (
        P(("dp", "expert"), None),
        P(("dp", "expert"), None),
        P("expert", None, "dp"),
        P("expert", None, "dp"),
        P("expert", "dp", None),
    )
    return jax.shard_map(body, mesh=mesh, in_specs=in_specs, out_specs=out_specs, check_vma=False)
```

```python
import jax
import jax.numpy as jnp
from jax import lax
from jax.sharding import PartitionSpec as P

LANES = 128


def ring_pairs(count, step):
    return [(i, (i + step) % count) for i in range(count)]


def ring_gather(x, axis):
    count = lax.axis_size(axis)
    fwd = ring_pairs(count, 1)
    bwd = ring_pairs(count, -1)
    half = x.shape[0] // 2
    from_prev = lax.ppermute(x, axis, fwd)
    from_next = lax.ppermute(x, axis, bwd)
    far_a = lax.ppermute(from_prev[:half], axis, fwd)
    far_b = lax.ppermute(from_next[half:], axis, bwd)
    return [x, from_next, jnp.concatenate([far_a, far_b], axis=0), from_prev]


def ring_reduce_scatter(blocks, axis, wire):
    count = lax.axis_size(axis)
    fwd = ring_pairs(count, 1)
    bwd = ring_pairs(count, -1)
    own, to_next, far, to_prev = blocks
    half = own.shape[0] // 2

    def send(x, pairs):
        return lax.ppermute(x.astype(wire), axis, pairs).astype(jnp.float32)

    direct_prev = send(to_next[half:], fwd)
    direct_next = send(to_prev[:half], bwd)
    got_a = send(far[:half], fwd)
    got_b = send(far[half:], bwd)
    relay_prev = send(to_next[:half] + got_a, fwd)
    relay_next = send(to_prev[half:] + got_b, bwd)
    return jnp.concatenate(
        [own[:half] + relay_prev + direct_next, own[half:] + direct_prev + relay_next], axis=0
    )


def body(tokens, out_grad, routes, gate_probs, w_gate, w_up, w_down):
    expert_count = lax.axis_size("expert")
    tok_count, width = tokens.shape
    top_count = routes.shape[1]
    capacity = 3 * tok_count * top_count // (2 * expert_count)
    slot_total = expert_count * capacity
    per_peer = capacity * width // LANES
    flat_routes = routes.reshape(-1)
    one_hot = (flat_routes[:, None] == jnp.arange(expert_count, dtype=jnp.int32)[None, :]).astype(
        jnp.int32
    )
    earlier = jnp.cumsum(one_hot, axis=0) - one_hot
    slot_index = jnp.sum(earlier * one_hot, axis=1)
    destination = flat_routes * capacity + slot_index
    placing = (jnp.arange(slot_total, dtype=jnp.int32)[:, None] == destination[None, :]).astype(
        jnp.bfloat16
    )
    collect = jnp.sum(placing.reshape(slot_total, tok_count, top_count), axis=2)
    sent_in = (
        jnp.dot(collect, tokens, preferred_element_type=jnp.float32)
        .astype(jnp.bfloat16)
        .reshape(expert_count, per_peer, LANES)
    )
    weighted = jnp.sum(
        placing.reshape(slot_total, tok_count, top_count) * gate_probs[None, :, :], axis=2
    )
    sent_dy = (
        jnp.dot(weighted, out_grad, preferred_element_type=jnp.float32)
        .astype(jnp.bfloat16)
        .reshape(expert_count, per_peer, LANES)
    )
    recv_in = lax.all_to_all(sent_in, "expert", 0, 0, tiled=True).reshape(slot_total, width)
    recv_dy = lax.all_to_all(sent_dy, "expert", 0, 0, tiled=True).reshape(slot_total, width)
    in_blocks = ring_gather(recv_in, "dp")
    dy_blocks = ring_gather(recv_dy, "dp")
    gate_w = w_gate[0]
    up_w = w_up[0]
    down_w = w_down[0]
    contract_last = (((1,), (1,)), ((), ()))
    contract_first = (((0,), (0,)), ((), ()))
    hidden_blocks = []
    gg_blocks = []
    gu_blocks = []
    row_blocks = []
    score_blocks = []
    for rows_in_k, rows_dy_k in zip(in_blocks, dy_blocks):
        gate_pre = jnp.dot(rows_in_k, gate_w, preferred_element_type=jnp.float32)
        up_pre = jnp.dot(rows_in_k, up_w, preferred_element_type=jnp.float32)
        sigmoid_gate = jax.nn.sigmoid(gate_pre)
        active = gate_pre * sigmoid_gate
        hidden = (active * up_pre).astype(jnp.bfloat16)
        back_hidden = lax.dot_general(
            rows_dy_k, down_w, contract_last, preferred_element_type=jnp.float32
        )
        score_blocks.append(jnp.sum(back_hidden * hidden.astype(jnp.float32), axis=1)[:, None])
        grad_gate_pre = (
            back_hidden * up_pre * sigmoid_gate * (1.0 + gate_pre * (1.0 - sigmoid_gate))
        ).astype(jnp.bfloat16)
        grad_up_pre = (back_hidden * active).astype(jnp.bfloat16)
        part = lax.dot_general(
            grad_gate_pre, gate_w, contract_last, preferred_element_type=jnp.float32
        )
        part = part + lax.dot_general(
            grad_up_pre, up_w, contract_last, preferred_element_type=jnp.float32
        )
        hidden_blocks.append(hidden)
        gg_blocks.append(grad_gate_pre)
        gu_blocks.append(grad_up_pre)
        row_blocks.append(part)
    own_grad = ring_reduce_scatter(row_blocks, "dp", jnp.bfloat16).astype(jnp.bfloat16)
    own_score = ring_reduce_scatter(score_blocks, "dp", jnp.float32).astype(jnp.bfloat16)
    rows_in = jnp.concatenate(in_blocks, axis=0)
    scaled = jnp.concatenate(dy_blocks, axis=0)
    hidden = jnp.concatenate(hidden_blocks, axis=0)
    grad_gate_pre = jnp.concatenate(gg_blocks, axis=0)
    grad_up_pre = jnp.concatenate(gu_blocks, axis=0)
    grad_down = lax.dot_general(
        hidden, scaled, contract_first, preferred_element_type=jnp.float32
    ).astype(jnp.bfloat16)
    grad_gate = lax.dot_general(
        rows_in, grad_gate_pre, contract_first, preferred_element_type=jnp.float32
    ).astype(jnp.bfloat16)
    grad_up = lax.dot_general(
        rows_in, grad_up_pre, contract_first, preferred_element_type=jnp.float32
    ).astype(jnp.bfloat16)
    own_rows = own_grad.reshape(expert_count, per_peer, LANES)
    own_scores = own_score.reshape(expert_count, 1, capacity)
    score_tile = jnp.pad(own_scores, ((0, 0), (0, 15), (0, LANES - capacity)))
    back_ext = lax.all_to_all(
        jnp.concatenate([own_rows, score_tile], axis=1), "expert", 0, 0, tiled=True
    )
    back_rows = back_ext[:, :per_peer].reshape(slot_total, width)
    back_scores = back_ext[:, per_peer, :capacity].reshape(slot_total)
    grad_tokens = lax.dot_general(
        collect, back_rows, contract_first, preferred_element_type=jnp.float32
    ).astype(jnp.bfloat16)
    weighted_scores = jnp.dot(back_scores, placing, preferred_element_type=jnp.float32)
    grad_probs = (
        (weighted_scores / gate_probs.reshape(-1).astype(jnp.float32))
        .astype(jnp.bfloat16)
        .reshape(tok_count, top_count)
    )
    return (grad_tokens, grad_probs, grad_gate[None], grad_up[None], grad_down[None])


def solution(mesh):
    in_specs = (
        P(("dp", "expert"), None),
        P(("dp", "expert"), None),
        P(("dp", "expert"), None),
        P(("dp", "expert"), None),
        P("expert", None, "dp"),
        P("expert", None, "dp"),
        P("expert", "dp", None),
    )
    out_specs = (
        P(("dp", "expert"), None),
        P(("dp", "expert"), None),
        P("expert", None, "dp"),
        P("expert", None, "dp"),
        P("expert", "dp", None),
    )
    return jax.shard_map(body, mesh=mesh, in_specs=in_specs, out_specs=out_specs, check_vma=False)
```

```python
import jax
import jax.numpy as jnp
from jax import lax
from jax.sharding import PartitionSpec as P

LANES = 128


def ring_pairs(count, step):
    return [(i, (i + step) % count) for i in range(count)]


def ring_gather(x, axis):
    count = lax.axis_size(axis)
    fwd = ring_pairs(count, 1)
    bwd = ring_pairs(count, -1)
    half = x.shape[0] // 2
    from_prev = lax.ppermute(x, axis, fwd)
    from_next = lax.ppermute(x, axis, bwd)
    far_a = lax.ppermute(from_prev[:half], axis, fwd)
    far_b = lax.ppermute(from_next[half:], axis, bwd)
    return jnp.concatenate([x, from_next, far_a, far_b, from_prev], axis=0)


def ring_reduce_scatter(blocks, axis, wire):
    count = lax.axis_size(axis)
    fwd = ring_pairs(count, 1)
    bwd = ring_pairs(count, -1)
    own, to_next, far, to_prev = blocks
    half = own.shape[0] // 2
    got_a = lax.ppermute(far[:half].astype(wire), axis, fwd).astype(jnp.float32)
    got_b = lax.ppermute(far[half:].astype(wire), axis, bwd).astype(jnp.float32)
    send_next = jnp.concatenate([to_next[:half] + got_a, to_next[half:]], axis=0)
    send_prev = jnp.concatenate([to_prev[:half], to_prev[half:] + got_b], axis=0)
    from_prev = lax.ppermute(send_next.astype(wire), axis, fwd).astype(jnp.float32)
    from_next = lax.ppermute(send_prev.astype(wire), axis, bwd).astype(jnp.float32)
    return own + from_prev + from_next


def body(tokens, out_grad, routes, gate_probs, w_gate, w_up, w_down):
    expert_count = lax.axis_size("expert")
    tok_count, width = tokens.shape
    top_count = routes.shape[1]
    capacity = 3 * tok_count * top_count // (2 * expert_count)
    slot_total = expert_count * capacity
    per_peer = capacity * width // LANES
    flat_routes = routes.reshape(-1)
    one_hot = (flat_routes[:, None] == jnp.arange(expert_count, dtype=jnp.int32)[None, :]).astype(
        jnp.int32
    )
    earlier = jnp.cumsum(one_hot, axis=0) - one_hot
    slot_index = jnp.sum(earlier * one_hot, axis=1)
    destination = flat_routes * capacity + slot_index
    placing = (jnp.arange(slot_total, dtype=jnp.int32)[:, None] == destination[None, :]).astype(
        jnp.bfloat16
    )
    collect = jnp.sum(placing.reshape(slot_total, tok_count, top_count), axis=2)
    sent_in = (
        jnp.dot(collect, tokens, preferred_element_type=jnp.float32)
        .astype(jnp.bfloat16)
        .reshape(expert_count, per_peer, LANES)
    )
    weighted = jnp.sum(
        placing.reshape(slot_total, tok_count, top_count) * gate_probs[None, :, :], axis=2
    )
    sent_dy = (
        jnp.dot(weighted, out_grad, preferred_element_type=jnp.float32)
        .astype(jnp.bfloat16)
        .reshape(expert_count, per_peer, LANES)
    )
    recv_in = lax.all_to_all(sent_in, "expert", 0, 0, tiled=True).reshape(slot_total, width)
    recv_dy = lax.all_to_all(sent_dy, "expert", 0, 0, tiled=True).reshape(slot_total, width)
    rows_in = ring_gather(recv_in, "dp")
    recv_dy, rows_in = lax.optimization_barrier((recv_dy, rows_in))
    rows_dy = ring_gather(recv_dy, "dp")
    gate_w = w_gate[0]
    up_w = w_up[0]
    down_w = w_down[0]
    contract_last = (((1,), (1,)), ((), ()))
    contract_first = (((0,), (0,)), ((), ()))
    gate_pre = jnp.dot(rows_in, gate_w, preferred_element_type=jnp.float32)
    up_pre = jnp.dot(rows_in, up_w, preferred_element_type=jnp.float32)
    sigmoid_gate = jax.nn.sigmoid(gate_pre)
    active = gate_pre * sigmoid_gate
    hidden = (active * up_pre).astype(jnp.bfloat16)
    back_hidden = lax.dot_general(
        rows_dy, down_w, contract_last, preferred_element_type=jnp.float32
    )
    score_part = jnp.sum(back_hidden * hidden.astype(jnp.float32), axis=1)
    scaled = rows_dy
    grad_gate_pre = (
        back_hidden * up_pre * sigmoid_gate * (1.0 + gate_pre * (1.0 - sigmoid_gate))
    ).astype(jnp.bfloat16)
    grad_up_pre = (back_hidden * active).astype(jnp.bfloat16)
    row_total = grad_gate_pre.shape[0]
    dp_count = lax.axis_size("dp")
    block = row_total // dp_count
    row_blocks = []
    for k in range(dp_count):
        rows = slice(k * block, (k + 1) * block)
        part = lax.dot_general(
            grad_gate_pre[rows], gate_w, contract_last, preferred_element_type=jnp.float32
        )
        part = part + lax.dot_general(
            grad_up_pre[rows], up_w, contract_last, preferred_element_type=jnp.float32
        )
        row_blocks.append(part)
    own_grad = ring_reduce_scatter(row_blocks, "dp", jnp.bfloat16).astype(jnp.bfloat16)
    score_blocks = [score_part[k * block:(k + 1) * block, None] for k in range(dp_count)]
    own_score = ring_reduce_scatter(score_blocks, "dp", jnp.float32).astype(jnp.bfloat16)
    grad_down = lax.dot_general(
        hidden, scaled, contract_first, preferred_element_type=jnp.float32
    ).astype(jnp.bfloat16)
    grad_gate = lax.dot_general(
        rows_in, grad_gate_pre, contract_first, preferred_element_type=jnp.float32
    ).astype(jnp.bfloat16)
    grad_up = lax.dot_general(
        rows_in, grad_up_pre, contract_first, preferred_element_type=jnp.float32
    ).astype(jnp.bfloat16)
    own_rows = own_grad.reshape(expert_count, per_peer, LANES)
    own_scores = own_score.reshape(expert_count, 1, capacity)
    score_tile = jnp.pad(own_scores, ((0, 0), (0, 15), (0, LANES - capacity)))
    back_ext = lax.all_to_all(
        jnp.concatenate([own_rows, score_tile], axis=1), "expert", 0, 0, tiled=True
    )
    back_rows = back_ext[:, :per_peer].reshape(slot_total, width)
    back_scores = back_ext[:, per_peer, :capacity].reshape(slot_total)
    grad_tokens = lax.dot_general(
        collect, back_rows, contract_first, preferred_element_type=jnp.float32
    ).astype(jnp.bfloat16)
    weighted_scores = jnp.dot(back_scores, placing, preferred_element_type=jnp.float32)
    grad_probs = (
        (weighted_scores / gate_probs.reshape(-1).astype(jnp.float32))
        .astype(jnp.bfloat16)
        .reshape(tok_count, top_count)
    )
    return (grad_tokens, grad_probs, grad_gate[None], grad_up[None], grad_down[None])


def solution(mesh):
    in_specs = (
        P(("dp", "expert"), None),
        P(("dp", "expert"), None),
        P(("dp", "expert"), None),
        P(("dp", "expert"), None),
        P("expert", None, "dp"),
        P("expert", None, "dp"),
        P("expert", "dp", None),
    )
    out_specs = (
        P(("dp", "expert"), None),
        P(("dp", "expert"), None),
        P("expert", None, "dp"),
        P("expert", None, "dp"),
        P("expert", "dp", None),
    )
    return jax.shard_map(body, mesh=mesh, in_specs=in_specs, out_specs=out_specs, check_vma=False)
```

```python
import jax
import jax.numpy as jnp
from jax import lax
from jax.sharding import PartitionSpec as P

LANES = 128


def ring_pairs(count, step):
    return [(i, (i + step) % count) for i in range(count)]


def ring_gather(x, axis):
    count = lax.axis_size(axis)
    fwd = ring_pairs(count, 1)
    bwd = ring_pairs(count, -1)
    half = x.shape[0] // 2
    from_prev = lax.ppermute(x, axis, fwd)
    from_next = lax.ppermute(x, axis, bwd)
    far_a = lax.ppermute(from_prev[:half], axis, fwd)
    far_b = lax.ppermute(from_next[half:], axis, bwd)
    return jnp.concatenate([x, from_next, far_a, far_b, from_prev], axis=0)


def ring_reduce_scatter(blocks, axis, wire):
    count = lax.axis_size(axis)
    fwd = ring_pairs(count, 1)
    bwd = ring_pairs(count, -1)
    own, to_next, far, to_prev = blocks
    half = own.shape[0] // 2
    got_a = lax.ppermute(far[:half].astype(wire), axis, fwd).astype(jnp.float32)
    got_b = lax.ppermute(far[half:].astype(wire), axis, bwd).astype(jnp.float32)
    send_next = jnp.concatenate([to_next[:half] + got_a, to_next[half:]], axis=0)
    send_prev = jnp.concatenate([to_prev[:half], to_prev[half:] + got_b], axis=0)
    from_prev = lax.ppermute(send_next.astype(wire), axis, fwd).astype(jnp.float32)
    from_next = lax.ppermute(send_prev.astype(wire), axis, bwd).astype(jnp.float32)
    return own + from_prev + from_next


def body(tokens, out_grad, routes, gate_probs, w_gate, w_up, w_down):
    expert_count = lax.axis_size("expert")
    tok_count, width = tokens.shape
    top_count = routes.shape[1]
    capacity = 3 * tok_count * top_count // (2 * expert_count)
    slot_total = expert_count * capacity
    per_peer = capacity * width // LANES
    flat_routes = routes.reshape(-1)
    one_hot = (flat_routes[:, None] == jnp.arange(expert_count, dtype=jnp.int32)[None, :]).astype(
        jnp.int32
    )
    earlier = jnp.cumsum(one_hot, axis=0) - one_hot
    slot_index = jnp.sum(earlier * one_hot, axis=1)
    destination = flat_routes * capacity + slot_index
    placing = (jnp.arange(slot_total, dtype=jnp.int32)[:, None] == destination[None, :]).astype(
        jnp.bfloat16
    )
    collect = jnp.sum(placing.reshape(slot_total, tok_count, top_count), axis=2)
    sent_in = (
        jnp.dot(collect, tokens, preferred_element_type=jnp.float32)
        .astype(jnp.bfloat16)
        .reshape(expert_count, per_peer, LANES)
    )
    weighted = jnp.sum(
        placing.reshape(slot_total, tok_count, top_count) * gate_probs[None, :, :], axis=2
    )
    sent_dy = (
        jnp.dot(weighted, out_grad, preferred_element_type=jnp.float32)
        .astype(jnp.bfloat16)
        .reshape(expert_count, per_peer, LANES)
    )
    recv_in = lax.all_to_all(sent_in, "expert", 0, 0, tiled=True).reshape(slot_total, width)
    recv_dy = lax.all_to_all(sent_dy, "expert", 0, 0, tiled=True).reshape(slot_total, width)
    rows_in = ring_gather(recv_in, "dp")
    rows_dy = ring_gather(recv_dy, "dp")
    gate_w = w_gate[0]
    up_w = w_up[0]
    down_w = w_down[0]
    contract_last = (((1,), (1,)), ((), ()))
    contract_first = (((0,), (0,)), ((), ()))
    gate_pre = jnp.dot(rows_in, gate_w, preferred_element_type=jnp.float32)
    up_pre = jnp.dot(rows_in, up_w, preferred_element_type=jnp.float32)
    sigmoid_gate = jax.nn.sigmoid(gate_pre)
    active = gate_pre * sigmoid_gate
    hidden = (active * up_pre).astype(jnp.bfloat16)
    back_hidden = lax.dot_general(
        rows_dy, down_w, contract_last, preferred_element_type=jnp.float32
    )
    score_part = jnp.sum(back_hidden * hidden.astype(jnp.float32), axis=1)
    scaled = rows_dy
    grad_gate_pre = (
        back_hidden * up_pre * sigmoid_gate * (1.0 + gate_pre * (1.0 - sigmoid_gate))
    ).astype(jnp.bfloat16)
    grad_up_pre = (back_hidden * active).astype(jnp.bfloat16)
    row_total = grad_gate_pre.shape[0]
    dp_count = lax.axis_size("dp")
    block = row_total // dp_count
    row_blocks = []
    for k in range(dp_count):
        rows = slice(k * block, (k + 1) * block)
        part = lax.dot_general(
            grad_gate_pre[rows], gate_w, contract_last, preferred_element_type=jnp.float32
        )
        part = part + lax.dot_general(
            grad_up_pre[rows], up_w, contract_last, preferred_element_type=jnp.float32
        )
        row_blocks.append(part)
    own_grad = ring_reduce_scatter(row_blocks, "dp", jnp.bfloat16).astype(jnp.bfloat16)
    score_blocks = [score_part[k * block:(k + 1) * block, None] for k in range(dp_count)]
    own_score = score_blocks[0]
    for k in range(1, dp_count):
        own_score = own_score + lax.ppermute(score_blocks[k], "dp", ring_pairs(dp_count, k))
    own_score = own_score.astype(jnp.bfloat16)
    grad_down = lax.dot_general(
        hidden, scaled, contract_first, preferred_element_type=jnp.float32
    ).astype(jnp.bfloat16)
    grad_gate = lax.dot_general(
        rows_in, grad_gate_pre, contract_first, preferred_element_type=jnp.float32
    ).astype(jnp.bfloat16)
    grad_up = lax.dot_general(
        rows_in, grad_up_pre, contract_first, preferred_element_type=jnp.float32
    ).astype(jnp.bfloat16)
    own_rows = own_grad.reshape(expert_count, per_peer, LANES)
    own_scores = own_score.reshape(expert_count, 1, capacity)
    score_tile = jnp.pad(own_scores, ((0, 0), (0, 15), (0, LANES - capacity)))
    back_ext = lax.all_to_all(
        jnp.concatenate([own_rows, score_tile], axis=1), "expert", 0, 0, tiled=True
    )
    back_rows = back_ext[:, :per_peer].reshape(slot_total, width)
    back_scores = back_ext[:, per_peer, :capacity].reshape(slot_total)
    grad_tokens = lax.dot_general(
        collect, back_rows, contract_first, preferred_element_type=jnp.float32
    ).astype(jnp.bfloat16)
    weighted_scores = jnp.dot(back_scores, placing, preferred_element_type=jnp.float32)
    grad_probs = (
        (weighted_scores / gate_probs.reshape(-1).astype(jnp.float32))
        .astype(jnp.bfloat16)
        .reshape(tok_count, top_count)
    )
    return (grad_tokens, grad_probs, grad_gate[None], grad_up[None], grad_down[None])


def solution(mesh):
    in_specs = (
        P(("dp", "expert"), None),
        P(("dp", "expert"), None),
        P(("dp", "expert"), None),
        P(("dp", "expert"), None),
        P("expert", None, "dp"),
        P("expert", None, "dp"),
        P("expert", "dp", None),
    )
    out_specs = (
        P(("dp", "expert"), None),
        P(("dp", "expert"), None),
        P("expert", None, "dp"),
        P("expert", None, "dp"),
        P("expert", "dp", None),
    )
    return jax.shard_map(body, mesh=mesh, in_specs=in_specs, out_specs=out_specs, check_vma=False)
```

```python
import jax
import jax.numpy as jnp
from jax import lax
from jax.sharding import PartitionSpec as P

LANES = 128


def ring_pairs(count, step):
    return [(i, (i + step) % count) for i in range(count)]


def ring_gather_blocks(x, axis):
    count = lax.axis_size(axis)
    fwd = ring_pairs(count, 1)
    bwd = ring_pairs(count, -1)
    half = x.shape[0] // 2
    from_prev = lax.ppermute(x, axis, fwd)
    from_next = lax.ppermute(x, axis, bwd)
    far_a = lax.ppermute(from_prev[:half], axis, fwd)
    far_b = lax.ppermute(from_next[half:], axis, bwd)
    return [x, from_next, jnp.concatenate([far_a, far_b], axis=0), from_prev]


def ring_gather(x, axis):
    count = lax.axis_size(axis)
    fwd = ring_pairs(count, 1)
    bwd = ring_pairs(count, -1)
    half = x.shape[0] // 2
    from_prev = lax.ppermute(x, axis, fwd)
    from_next = lax.ppermute(x, axis, bwd)
    far_a = lax.ppermute(from_prev[:half], axis, fwd)
    far_b = lax.ppermute(from_next[half:], axis, bwd)
    return jnp.concatenate([x, from_next, far_a, far_b, from_prev], axis=0)


def ring_reduce_scatter(blocks, axis, wire):
    count = lax.axis_size(axis)
    fwd = ring_pairs(count, 1)
    bwd = ring_pairs(count, -1)
    own, to_next, far, to_prev = blocks
    half = own.shape[0] // 2
    got_a = lax.ppermute(far[:half].astype(wire), axis, fwd).astype(jnp.float32)
    got_b = lax.ppermute(far[half:].astype(wire), axis, bwd).astype(jnp.float32)
    send_next = jnp.concatenate([to_next[:half] + got_a, to_next[half:]], axis=0)
    send_prev = jnp.concatenate([to_prev[:half], to_prev[half:] + got_b], axis=0)
    from_prev = lax.ppermute(send_next.astype(wire), axis, fwd).astype(jnp.float32)
    from_next = lax.ppermute(send_prev.astype(wire), axis, bwd).astype(jnp.float32)
    return own + from_prev + from_next


def body(tokens, out_grad, routes, gate_probs, w_gate, w_up, w_down):
    expert_count = lax.axis_size("expert")
    tok_count, width = tokens.shape
    top_count = routes.shape[1]
    capacity = 3 * tok_count * top_count // (2 * expert_count)
    slot_total = expert_count * capacity
    per_peer = capacity * width // LANES
    flat_routes = routes.reshape(-1)
    one_hot = (flat_routes[:, None] == jnp.arange(expert_count, dtype=jnp.int32)[None, :]).astype(
        jnp.int32
    )
    earlier = jnp.cumsum(one_hot, axis=0) - one_hot
    slot_index = jnp.sum(earlier * one_hot, axis=1)
    destination = flat_routes * capacity + slot_index
    placing = (jnp.arange(slot_total, dtype=jnp.int32)[:, None] == destination[None, :]).astype(
        jnp.bfloat16
    )
    collect = jnp.sum(placing.reshape(slot_total, tok_count, top_count), axis=2)
    sent_in = (
        jnp.dot(collect, tokens, preferred_element_type=jnp.float32)
        .astype(jnp.bfloat16)
        .reshape(expert_count, per_peer, LANES)
    )
    weighted = jnp.sum(
        placing.reshape(slot_total, tok_count, top_count) * gate_probs[None, :, :], axis=2
    )
    sent_dy = (
        jnp.dot(weighted, out_grad, preferred_element_type=jnp.float32)
        .astype(jnp.bfloat16)
        .reshape(expert_count, per_peer, LANES)
    )
    recv_in = lax.all_to_all(sent_in, "expert", 0, 0, tiled=True).reshape(slot_total, width)
    recv_dy = lax.all_to_all(sent_dy, "expert", 0, 0, tiled=True).reshape(slot_total, width)
    in_blocks = ring_gather_blocks(recv_in, "dp")
    rows_in = jnp.concatenate(in_blocks, axis=0)
    rows_dy = ring_gather(recv_dy, "dp")
    gate_w = w_gate[0]
    up_w = w_up[0]
    down_w = w_down[0]
    contract_last = (((1,), (1,)), ((), ()))
    contract_first = (((0,), (0,)), ((), ()))
    gate_pre = jnp.concatenate(
        [jnp.dot(b, gate_w, preferred_element_type=jnp.float32) for b in in_blocks], axis=0
    )
    up_pre = jnp.concatenate(
        [jnp.dot(b, up_w, preferred_element_type=jnp.float32) for b in in_blocks], axis=0
    )
    sigmoid_gate = jax.nn.sigmoid(gate_pre)
    active = gate_pre * sigmoid_gate
    hidden = (active * up_pre).astype(jnp.bfloat16)
    back_hidden = lax.dot_general(
        rows_dy, down_w, contract_last, preferred_element_type=jnp.float32
    )
    score_part = jnp.sum(back_hidden * hidden.astype(jnp.float32), axis=1)
    scaled = rows_dy
    grad_gate_pre = (
        back_hidden * up_pre * sigmoid_gate * (1.0 + gate_pre * (1.0 - sigmoid_gate))
    ).astype(jnp.bfloat16)
    grad_up_pre = (back_hidden * active).astype(jnp.bfloat16)
    row_total = grad_gate_pre.shape[0]
    dp_count = lax.axis_size("dp")
    block = row_total // dp_count
    row_blocks = []
    for k in range(dp_count):
        rows = slice(k * block, (k + 1) * block)
        part = lax.dot_general(
            grad_gate_pre[rows], gate_w, contract_last, preferred_element_type=jnp.float32
        )
        part = part + lax.dot_general(
            grad_up_pre[rows], up_w, contract_last, preferred_element_type=jnp.float32
        )
        row_blocks.append(part)
    own_grad = ring_reduce_scatter(row_blocks, "dp", jnp.bfloat16).astype(jnp.bfloat16)
    score_blocks = [score_part[k * block:(k + 1) * block, None] for k in range(dp_count)]
    own_score = score_blocks[0]
    for k in range(1, dp_count):
        own_score = own_score + lax.ppermute(score_blocks[k], "dp", ring_pairs(dp_count, k))
    own_score = own_score.astype(jnp.bfloat16)
    grad_down = lax.dot_general(
        hidden, scaled, contract_first, preferred_element_type=jnp.float32
    ).astype(jnp.bfloat16)
    grad_gate = lax.dot_general(
        rows_in, grad_gate_pre, contract_first, preferred_element_type=jnp.float32
    ).astype(jnp.bfloat16)
    grad_up = lax.dot_general(
        rows_in, grad_up_pre, contract_first, preferred_element_type=jnp.float32
    ).astype(jnp.bfloat16)
    own_rows = own_grad.reshape(expert_count, per_peer, LANES)
    own_scores = own_score.reshape(expert_count, 1, capacity)
    score_tile = jnp.pad(own_scores, ((0, 0), (0, 15), (0, LANES - capacity)))
    back_ext = lax.all_to_all(
        jnp.concatenate([own_rows, score_tile], axis=1), "expert", 0, 0, tiled=True
    )
    back_rows = back_ext[:, :per_peer].reshape(slot_total, width)
    back_scores = back_ext[:, per_peer, :capacity].reshape(slot_total)
    grad_tokens = lax.dot_general(
        collect, back_rows, contract_first, preferred_element_type=jnp.float32
    ).astype(jnp.bfloat16)
    weighted_scores = jnp.dot(back_scores, placing, preferred_element_type=jnp.float32)
    grad_probs = (
        (weighted_scores / gate_probs.reshape(-1).astype(jnp.float32))
        .astype(jnp.bfloat16)
        .reshape(tok_count, top_count)
    )
    return (grad_tokens, grad_probs, grad_gate[None], grad_up[None], grad_down[None])


def solution(mesh):
    in_specs = (
        P(("dp", "expert"), None),
        P(("dp", "expert"), None),
        P(("dp", "expert"), None),
        P(("dp", "expert"), None),
        P("expert", None, "dp"),
        P("expert", None, "dp"),
        P("expert", "dp", None),
    )
    out_specs = (
        P(("dp", "expert"), None),
        P(("dp", "expert"), None),
        P("expert", None, "dp"),
        P("expert", None, "dp"),
        P("expert", "dp", None),
    )
    return jax.shard_map(body, mesh=mesh, in_specs=in_specs, out_specs=out_specs, check_vma=False)
```
